32 devices in a mesh: tm: 2 (over x), state: 16 (over z, y, core).
Axes of the slice: x: 2, y: 2, z: 4, core: 2. Of those that a mesh axis runs over, the one named last changes fastest.
Arguments:
- anomalies: bfloat16 [4, 24576, 256], P('tm', 'state'), may hold values from -23 to 23, as said below
- obs_weight: float32 [4, 24576], P('tm', 'state'), may hold values from 0.05 to 6, as said below
Outputs:
- smoothed: bfloat16 [4, 24576, 256], P('tm', 'state')
- suffix: float32 [4, 256, 256], P('tm')
The draws below stay inside these ranges and needn't reach their ends.
Inputs may be any that keep to these rules, and one draw needn't show every extreme that they name: Member anomalies of order one, with member columns correlated. `obs_weight`: positive weights.
All inputs are finite; a program needn't handle non-finite values. Where the reference program divides by a largest or mean magnitude, that divisor is 1e-20 or more.
Results may differ from the reference program's by a relative error of at most 0.001.
The reference program's roundings to bfloat16 on the way (of `weighted`) count: a program that leaves them out, or rounds other values in their place, can miss the bound.
Values sent between devices are 32-bit elements; how exact they have to be, the bound alone decides.
No kernel may reach another device: no remote copies, remote signals or barrier semaphores. Data moves between devices by JAX's collectives and lax.ppermute only.
A program may use at most 64 MiB of HBM per device.

```python
import jax
import jax.numpy as jnp
from jax import lax

MEMBERS = 256
NS_STEPS = 4
TIMES = 4
ROWS = 24576


def draw_anomalies(key, part):
    shifts = jax.random.randint(jax.random.fold_in(key, 11), (2,), 1, MEMBERS)
    base = jnp.clip(jax.random.normal(jax.random.fold_in(key, 12), (TIMES, ROWS, MEMBERS), jnp.float32), -5.0, 5.0)
    spread = jax.random.uniform(jax.random.fold_in(key, 13), (TIMES, ROWS, 1), jnp.float32, -0.7, 0.7)
    mixed = base + 0.7 * jnp.roll(base, shifts[0], axis=2) + 0.5 * jnp.roll(base, shifts[1], axis=2)
    return (jnp.exp(spread) * mixed).astype(jnp.bfloat16)


def draw_obs_weight(key, part):
    spread = jax.random.uniform(jax.random.fold_in(key, 21), (TIMES, ROWS), jnp.float32, -0.7, 0.7)
    position = jnp.arange(ROWS, dtype=jnp.float32) / ROWS
    rising = jnp.exp(jnp.log(3.0) * (position - 0.5))
    return (jnp.exp(spread) * rising[None, :]).astype(jnp.float32)


def setup_inputs(seed: int = 0) -> dict:
    streams_of = jax.random.split(jax.random.key(seed), 3)
    anomalies = draw_anomalies(jax.random.fold_in(streams_of[2], 71), 0)
    obs_weight = draw_obs_weight(jax.random.fold_in(streams_of[2], 71), 0)
    return {"anomalies": anomalies, "obs_weight": obs_weight}


def newton_root(covariance):
    identity = jnp.eye(covariance.shape[-1], dtype=jnp.float32)
    row_bound = lax.optimization_barrier(jnp.max(lax.optimization_barrier(jnp.sum(jnp.abs(covariance), axis=-1)), axis=-1))
    iterate = covariance / row_bound[:, None, None]
    inverse_root = jnp.broadcast_to(identity, covariance.shape)
    for sweep_index in range(NS_STEPS):
        factor = 1.5 * identity - 0.5 * jnp.matmul(inverse_root, iterate, precision=lax.Precision.HIGHEST)
        iterate = jnp.matmul(iterate, factor, precision=lax.Precision.HIGHEST)
        inverse_root = jnp.matmul(factor, inverse_root, precision=lax.Precision.HIGHEST)
    return inverse_root / jnp.sqrt(row_bound)[:, None, None]

def reference(anomalies, obs_weight):
    grams = []
    for time_index in range(TIMES):
        weighted = (anomalies[time_index] * obs_weight[time_index][:, None]).astype(jnp.bfloat16)
        grams.append(jnp.dot(weighted.T, weighted, preferred_element_type=jnp.float32))
    gram = jnp.stack(grams) / ROWS
    covariance = gram + jnp.eye(MEMBERS, dtype=jnp.float32)
    transform = newton_root(covariance)
    product = transform[TIMES - 1]
    suffixes = [product]
    for time_index in range(TIMES - 2, -1, -1):
        product = jnp.matmul(transform[time_index], product, precision=lax.Precision.HIGHEST)
        suffixes.append(product)
    suffix = jnp.stack(suffixes[::-1])
    outputs = []
    for time_index in range(TIMES):
        outputs.append(jnp.dot(anomalies[time_index], suffix[time_index].astype(jnp.bfloat16), preferred_element_type=jnp.float32).astype(jnp.bfloat16))
    smoothed = jnp.stack(outputs)
    return (smoothed, suffix)
```

```python
import jax
import jax.numpy as jnp
from jax import lax
from jax.sharding import PartitionSpec as P

NS_STEPS = 4
HI = lax.Precision.HIGHEST


def xor_pairs(count, stride):
    return [(source, source ^ stride) for source in range(count)]


def strides_of(count):
    out, stride = [], 1
    while stride < count:
        out.append(stride)
        stride *= 2
    return out


def halving_sum(value, axis):
    count, me = lax.axis_size(axis), lax.axis_index(axis)
    strides = strides_of(count)
    rows = value.shape[0]
    padded = -(-rows // count) * count
    if padded != rows:
        value = jnp.concatenate([value, jnp.zeros((padded - rows,) + value.shape[1:], value.dtype)])
    for stride in strides:
        upper = (me // stride) % 2 == 1
        half = value.shape[0] // 2
        low, high = value[:half], value[half:]
        send = jnp.where(upper, low, high)
        keep = jnp.where(upper, high, low)
        value = keep + lax.ppermute(send, axis, xor_pairs(count, stride))
    for stride in strides[::-1]:
        upper = (me // stride) % 2 == 1
        other = lax.ppermute(value, axis, xor_pairs(count, stride))
        value = jnp.where(upper, jnp.concatenate([other, value]), jnp.concatenate([value, other]))
    return value[:rows]


def state_sum(partial_gram, axis):
    times, n, _ = partial_gram.shape
    return halving_sum(partial_gram.reshape(times * n, n), axis).reshape(times, n, n)


def newton_root(covariance):
    identity = jnp.eye(covariance.shape[-1], dtype=jnp.float32)
    row_bound = jnp.max(jnp.sum(jnp.abs(covariance), axis=-1), axis=-1)
    iterate = covariance / row_bound[:, None, None]
    inverse_root = jnp.broadcast_to(identity, covariance.shape)
    for sweep_index in range(NS_STEPS):
        factor = 1.5 * identity - 0.5 * jnp.matmul(inverse_root, iterate, precision=HI)
        iterate = jnp.matmul(iterate, factor, precision=HI)
        inverse_root = jnp.matmul(factor, inverse_root, precision=HI)
    return inverse_root / jnp.sqrt(row_bound)[:, None, None]


def later_product(local, axis):
    count, me = lax.axis_size(axis), lax.axis_index(axis)
    identity = jnp.eye(local.shape[-1], dtype=local.dtype)
    if count == 1:
        return identity
    shifted = lax.ppermute(local, axis, [(j, j - 1) for j in range(1, count)])
    carried = jnp.where(me + 1 < count, shifted, identity)
    reach = 1
    while reach < count - 1:
        further = lax.ppermute(carried, axis, [(j, j - reach) for j in range(reach, count)])
        further = jnp.where(me + reach < count, further, identity)
        carried = jnp.matmul(carried, further, precision=HI)
        reach *= 2
    return carried


def on_device(anomalies, obs_weight):
    times_dev, rows_dev, members = anomalies.shape
    total_rows = rows_dev * lax.axis_size("state")
    weighted = (anomalies * obs_weight[:, :, None]).astype(jnp.bfloat16)
    partial_gram = jnp.einsum("trm,trn->tmn", weighted, weighted, preferred_element_type=jnp.float32)
    gram_sum = state_sum(partial_gram, "state")
    covariance = gram_sum / total_rows + jnp.eye(members, dtype=jnp.float32)
    transform = newton_root(covariance)
    local_product = transform[times_dev - 1]
    for time_index in range(times_dev - 2, -1, -1):
        local_product = jnp.matmul(transform[time_index], local_product, precision=HI)
    product = later_product(local_product, "tm")
    suffixes = []
    for time_index in range(times_dev - 1, -1, -1):
        product = jnp.matmul(transform[time_index], product, precision=HI)
        suffixes.append(product)
    suffix = jnp.stack(suffixes[::-1])
    smoothed = jnp.einsum("trm,tmn->trn", anomalies, suffix.astype(jnp.bfloat16), preferred_element_type=jnp.float32).astype(jnp.bfloat16)
    return (smoothed, suffix)


def solution(mesh):
    placed = (P("tm", "state", None), P("tm", "state"))
    return jax.shard_map(on_device, mesh=mesh, in_specs=placed, out_specs=(P("tm", "state", None), P("tm", None, None)), check_vma=False)
```

```python
import jax
import jax.numpy as jnp
from jax import lax
from jax.sharding import PartitionSpec as P

NS_STEPS = 4
HI = lax.Precision.HIGH
CHIP_RADIX = 4


def radix_plan(count):
    plan, place = [], 1
    if count % 2 == 0 and count > 1:
        plan.append((2, 1))
        place = 2
    while place < count:
        radix = min(CHIP_RADIX, count // place)
        plan.append((radix, place))
        place *= radix
    return plan


def digit_pairs(count, radix, place, offset):
    pairs = []
    for source in range(count):
        digit = (source // place) % radix
        pairs.append((source, source + (((digit + offset) % radix) - digit) * place))
    return pairs


def grouped_sum(value, axis):
    count, me = lax.axis_size(axis), lax.axis_index(axis)
    plan = radix_plan(count)
    rows = value.shape[0]
    for radix, place in plan:
        digit = (me // place) % radix
        if radix == 2:
            upper = digit == 1
            half = value.shape[0] // 2
            low, high = value[:half], value[half:]
            send, keep = jnp.where(upper, low, high), jnp.where(upper, high, low)
            value = keep + lax.ppermute(send, axis, digit_pairs(count, radix, place, 1))
            continue
        chunk = value.shape[0] // radix
        pieces = value.reshape((radix, chunk) + value.shape[1:])
        total = lax.dynamic_index_in_dim(pieces, digit, 0, keepdims=False)
        for offset in range(1, radix):
            send = lax.dynamic_index_in_dim(pieces, (digit + offset) % radix, 0, keepdims=False)
            total = total + lax.ppermute(send, axis, digit_pairs(count, radix, place, offset))
        value = total
    for radix, place in plan[::-1]:
        digit = (me // place) % radix
        if radix == 2:
            other = lax.ppermute(value, axis, digit_pairs(count, radix, place, 1))
            value = jnp.where(digit == 1, jnp.concatenate([other, value]), jnp.concatenate([value, other]))
            continue
        got = [value] + [lax.ppermute(value, axis, digit_pairs(count, radix, place, offset)) for offset in range(1, radix)]
        stacked = jnp.stack(got)
        order = (digit - jnp.arange(radix)) % radix
        value = jnp.take(stacked, order, axis=0).reshape((radix * value.shape[0],) + value.shape[1:])
    return value


def state_sum(partial_gram, axis):
    times, n, _ = partial_gram.shape
    return grouped_sum(partial_gram.reshape(times * n, n), axis).reshape(times, n, n)


def newton_root(covariance):
    identity = jnp.eye(covariance.shape[-1], dtype=jnp.float32)
    row_bound = jnp.max(jnp.sum(jnp.abs(covariance), axis=-1), axis=-1)
    iterate = covariance / row_bound[:, None, None]
    inverse_root = jnp.broadcast_to(identity, covariance.shape)
    for sweep_index in range(NS_STEPS):
        factor = 1.5 * identity - 0.5 * jnp.matmul(inverse_root, iterate, precision=HI)
        iterate = jnp.matmul(iterate, factor, precision=HI)
        inverse_root = jnp.matmul(factor, inverse_root, precision=HI)
    return inverse_root / jnp.sqrt(row_bound)[:, None, None]


def later_product(local, axis):
    count, me = lax.axis_size(axis), lax.axis_index(axis)
    identity = jnp.eye(local.shape[-1], dtype=local.dtype)
    if count == 1:
        return identity
    shifted = lax.ppermute(local, axis, [(j, j - 1) for j in range(1, count)])
    carried = jnp.where(me + 1 < count, shifted, identity)
    reach = 1
    while reach < count - 1:
        further = lax.ppermute(carried, axis, [(j, j - reach) for j in range(reach, count)])
        further = jnp.where(me + reach < count, further, identity)
        carried = jnp.matmul(carried, further, precision=HI)
        reach *= 2
    return carried


def on_device(anomalies, obs_weight):
    times_dev, rows_dev, members = anomalies.shape
    total_rows = rows_dev * lax.axis_size("state")
    weighted = (anomalies * obs_weight[:, :, None]).astype(jnp.bfloat16)
    partial_gram = jnp.einsum("trm,trn->tmn", weighted, weighted, preferred_element_type=jnp.float32)
    gram_sum = state_sum(partial_gram, "state")
    covariance = gram_sum / total_rows + jnp.eye(members, dtype=jnp.float32)
    transform = newton_root(covariance)
    local_product = transform[times_dev - 1]
    for time_index in range(times_dev - 2, -1, -1):
        local_product = jnp.matmul(transform[time_index], local_product, precision=HI)
    product = later_product(local_product, "tm")
    suffixes = []
    for time_index in range(times_dev - 1, -1, -1):
        product = jnp.matmul(transform[time_index], product, precision=HI)
        suffixes.append(product)
    suffix = jnp.stack(suffixes[::-1])
    smoothed = jnp.einsum("trm,tmn->trn", anomalies, suffix.astype(jnp.bfloat16), preferred_element_type=jnp.float32).astype(jnp.bfloat16)
    return (smoothed, suffix)


def solution(mesh):
    placed = (P("tm", "state", None), P("tm", "state"))
    return jax.shard_map(on_device, mesh=mesh, in_specs=placed, out_specs=(P("tm", "state", None), P("tm", None, None)), check_vma=False)
```

```python
import jax
import jax.numpy as jnp
from jax import lax
from jax.sharding import PartitionSpec as P
from jax.experimental import pallas as pl
from jax.experimental.pallas import tpu as pltpu

NS_STEPS = 4
HI = lax.Precision.HIGH
CHIP_RADIX = 4
SPLIT = True
PALLAS_SMOOTH = True


def radix_plan(count):
    plan, place = [], 1
    if count % 2 == 0 and count > 1:
        plan.append((2, 1))
        place = 2
    while place < count:
        radix = min(CHIP_RADIX, count // place)
        plan.append((radix, place))
        place *= radix
    return plan


def digit_pairs(count, radix, place, offset):
    pairs = []
    for source in range(count):
        digit = (source // place) % radix
        pairs.append((source, source + (((digit + offset) % radix) - digit) * place))
    return pairs


def grouped_sum(value, axis):
    count, me = lax.axis_size(axis), lax.axis_index(axis)
    plan = radix_plan(count)
    rows = value.shape[0]
    for radix, place in plan:
        digit = (me // place) % radix
        if radix == 2:
            upper = digit == 1
            half = value.shape[0] // 2
            low, high = value[:half], value[half:]
            send, keep = jnp.where(upper, low, high), jnp.where(upper, high, low)
            value = keep + lax.ppermute(send, axis, digit_pairs(count, radix, place, 1))
            continue
        chunk = value.shape[0] // radix
        pieces = value.reshape((radix, chunk) + value.shape[1:])
        total = lax.dynamic_index_in_dim(pieces, digit, 0, keepdims=False)
        for offset in range(1, radix):
            send = lax.dynamic_index_in_dim(pieces, (digit + offset) % radix, 0, keepdims=False)
            total = total + lax.ppermute(send, axis, digit_pairs(count, radix, place, offset))
        value = total
    for radix, place in plan[::-1]:
        digit = (me // place) % radix
        if radix == 2:
            other = lax.ppermute(value, axis, digit_pairs(count, radix, place, 1))
            value = jnp.where(digit == 1, jnp.concatenate([other, value]), jnp.concatenate([value, other]))
            continue
        got = [value] + [lax.ppermute(value, axis, digit_pairs(count, radix, place, offset)) for offset in range(1, radix)]
        stacked = jnp.stack(got)
        order = (digit - jnp.arange(radix)) % radix
        value = jnp.take(stacked, order, axis=0).reshape((radix * value.shape[0],) + value.shape[1:])
    return value


def state_sum(partial_gram, axis):
    times, n, _ = partial_gram.shape
    return grouped_sum(partial_gram.reshape(times * n, n), axis).reshape(times, n, n)


def newton_root(covariance):
    identity = jnp.eye(covariance.shape[-1], dtype=jnp.float32)
    row_bound = jnp.max(jnp.sum(jnp.abs(covariance), axis=-1), axis=-1)
    iterate = covariance / row_bound[:, None, None]
    inverse_root = jnp.broadcast_to(identity, covariance.shape)
    for sweep_index in range(NS_STEPS):
        factor = 1.5 * identity - 0.5 * jnp.matmul(inverse_root, iterate, precision=HI)
        iterate = jnp.matmul(iterate, factor, precision=HI)
        inverse_root = jnp.matmul(factor, inverse_root, precision=HI)
    return inverse_root / jnp.sqrt(row_bound)[:, None, None]


def split_shift(value, axis, pairs):
    count = lax.axis_size("state")
    if not SPLIT or count % 2:
        return lax.ppermute(value, axis, pairs)
    upper = lax.axis_index("state") % 2 == 1
    half = value.shape[0] // 2
    part = jnp.where(upper, value[half:], value[:half])
    got = lax.ppermute(part, axis, pairs)
    other = lax.ppermute(got, "state", digit_pairs(count, 2, 1, 1))
    return jnp.where(upper, jnp.concatenate([other, got]), jnp.concatenate([got, other]))


def later_product(local, axis):
    count, me = lax.axis_size(axis), lax.axis_index(axis)
    identity = jnp.eye(local.shape[-1], dtype=local.dtype)
    if count == 1:
        return identity
    shifted = split_shift(local, axis, [(j, j - 1) for j in range(1, count)])
    carried = jnp.where(me + 1 < count, shifted, identity)
    reach = 1
    while reach < count - 1:
        further = split_shift(carried, axis, [(j, j - reach) for j in range(reach, count)])
        further = jnp.where(me + reach < count, further, identity)
        carried = jnp.matmul(carried, further, precision=HI)
        reach *= 2
    return carried


def smooth_kernel(anomaly_ref, suffix_ref, out_ref):
    out_ref[0] = jnp.dot(anomaly_ref[0], suffix_ref[0].astype(jnp.bfloat16), preferred_element_type=jnp.float32).astype(out_ref.dtype)


def smooth(anomalies, suffix):
    times, rows, members = anomalies.shape
    return pl.pallas_call(
        smooth_kernel,
        out_shape=jax.ShapeDtypeStruct(anomalies.shape, anomalies.dtype),
        grid=(times,),
        in_specs=[pl.BlockSpec((1, rows, members), lambda t: (t, 0, 0)), pl.BlockSpec((1, members, members), lambda t: (t, 0, 0))],
        out_specs=pl.BlockSpec((1, rows, members), lambda t: (t, 0, 0)),
        cost_estimate=pl.CostEstimate(flops=2 * times * rows * members * members, transcendentals=0, bytes_accessed=2 * anomalies.size * 2 + suffix.size * 4),
    )(anomalies, suffix)


def on_device(anomalies, obs_weight):
    times_dev, rows_dev, members = anomalies.shape
    total_rows = rows_dev * lax.axis_size("state")
    weighted = (anomalies * obs_weight[:, :, None]).astype(jnp.bfloat16)
    partial_gram = jnp.einsum("trm,trn->tmn", weighted, weighted, preferred_element_type=jnp.float32)
    gram_sum = state_sum(partial_gram, "state")
    covariance = gram_sum / total_rows + jnp.eye(members, dtype=jnp.float32)
    transform = newton_root(covariance)
    local_product = transform[times_dev - 1]
    for time_index in range(times_dev - 2, -1, -1):
        local_product = jnp.matmul(transform[time_index], local_product, precision=HI)
    product = later_product(local_product, "tm")
    suffixes = []
    for time_index in range(times_dev - 1, -1, -1):
        product = jnp.matmul(transform[time_index], product, precision=HI)
        suffixes.append(product)
    suffix = jnp.stack(suffixes[::-1])
    if PALLAS_SMOOTH:
        smoothed = smooth(anomalies, suffix)
    else:
        smoothed = jnp.einsum("trm,tmn->trn", anomalies, suffix.astype(jnp.bfloat16), preferred_element_type=jnp.float32).astype(jnp.bfloat16)
    return (smoothed, suffix)


def solution(mesh):
    placed = (P("tm", "state", None), P("tm", "state"))
    return jax.shard_map(on_device, mesh=mesh, in_specs=placed, out_specs=(P("tm", "state", None), P("tm", None, None)), check_vma=False)
```

```python
import jax
import jax.numpy as jnp
from jax import lax
from jax.sharding import PartitionSpec as P
from jax.experimental import pallas as pl
from jax.experimental.pallas import tpu as pltpu

NS_STEPS = 4
HI = lax.Precision.HIGHEST
NS_PRECISION = lax.Precision.HIGH
CHIP_RADIX = 4
SPLIT = True
PALLAS_SMOOTH = True


def radix_plan(count):
    plan, place = [], 1
    if count % 2 == 0 and count > 1:
        plan.append((2, 1))
        place = 2
    while place < count:
        radix = min(CHIP_RADIX, count // place)
        plan.append((radix, place))
        place *= radix
    return plan


def digit_pairs(count, radix, place, offset):
    pairs = []
    for source in range(count):
        digit = (source // place) % radix
        pairs.append((source, source + (((digit + offset) % radix) - digit) * place))
    return pairs


def grouped_sum(value, axis):
    count, me = lax.axis_size(axis), lax.axis_index(axis)
    plan = radix_plan(count)
    rows = value.shape[0]
    for radix, place in plan:
        digit = (me // place) % radix
        if radix == 2:
            upper = digit == 1
            half = value.shape[0] // 2
            low, high = value[:half], value[half:]
            send, keep = jnp.where(upper, low, high), jnp.where(upper, high, low)
            value = keep + lax.ppermute(send, axis, digit_pairs(count, radix, place, 1))
            continue
        chunk = value.shape[0] // radix
        pieces = value.reshape((radix, chunk) + value.shape[1:])
        total = lax.dynamic_index_in_dim(pieces, digit, 0, keepdims=False)
        for offset in range(1, radix):
            send = lax.dynamic_index_in_dim(pieces, (digit + offset) % radix, 0, keepdims=False)
            total = total + lax.ppermute(send, axis, digit_pairs(count, radix, place, offset))
        value = total
    for radix, place in plan[::-1]:
        digit = (me // place) % radix
        if radix == 2:
            other = lax.ppermute(value, axis, digit_pairs(count, radix, place, 1))
            value = jnp.where(digit == 1, jnp.concatenate([other, value]), jnp.concatenate([value, other]))
            continue
        got = [value] + [lax.ppermute(value, axis, digit_pairs(count, radix, place, offset)) for offset in range(1, radix)]
        stacked = jnp.stack(got)
        order = (digit - jnp.arange(radix)) % radix
        value = jnp.take(stacked, order, axis=0).reshape((radix * value.shape[0],) + value.shape[1:])
    return value


def state_sum(partial_gram, axis):
    times, n, _ = partial_gram.shape
    return grouped_sum(partial_gram.reshape(times * n, n), axis).reshape(times, n, n)


def newton_root(covariance):
    identity = jnp.eye(covariance.shape[-1], dtype=jnp.float32)
    row_bound = jnp.max(jnp.sum(jnp.abs(covariance), axis=-1), axis=-1)
    iterate = covariance / row_bound[:, None, None]
    inverse_root = jnp.broadcast_to(identity, covariance.shape)
    for sweep_index in range(NS_STEPS):
        factor = 1.5 * identity - 0.5 * jnp.matmul(inverse_root, iterate, precision=NS_PRECISION)
        iterate = jnp.matmul(iterate, factor, precision=NS_PRECISION)
        inverse_root = jnp.matmul(factor, inverse_root, precision=NS_PRECISION)
    return inverse_root / jnp.sqrt(row_bound)[:, None, None]


def split_shift(value, axis, pairs):
    count = lax.axis_size("state")
    if not SPLIT or count % 2:
        return lax.ppermute(value, axis, pairs)
    upper = lax.axis_index("state") % 2 == 1
    half = value.shape[0] // 2
    part = jnp.where(upper, value[half:], value[:half])
    got = lax.ppermute(part, axis, pairs)
    other = lax.ppermute(got, "state", digit_pairs(count, 2, 1, 1))
    return jnp.where(upper, jnp.concatenate([other, got]), jnp.concatenate([got, other]))


def later_product(local, axis):
    count, me = lax.axis_size(axis), lax.axis_index(axis)
    identity = jnp.eye(local.shape[-1], dtype=local.dtype)
    if count == 1:
        return identity
    shifted = split_shift(local, axis, [(j, j - 1) for j in range(1, count)])
    carried = jnp.where(me + 1 < count, shifted, identity)
    reach = 1
    while reach < count - 1:
        further = split_shift(carried, axis, [(j, j - reach) for j in range(reach, count)])
        further = jnp.where(me + reach < count, further, identity)
        carried = jnp.matmul(carried, further, precision=HI)
        reach *= 2
    return carried


def smooth_kernel(anomaly_ref, suffix_ref, out_ref):
    out_ref[0] = jnp.dot(anomaly_ref[0], suffix_ref[0].astype(jnp.bfloat16), preferred_element_type=jnp.float32).astype(out_ref.dtype)


def smooth(anomalies, suffix):
    times, rows, members = anomalies.shape
    return pl.pallas_call(
        smooth_kernel,
        out_shape=jax.ShapeDtypeStruct(anomalies.shape, anomalies.dtype),
        grid=(times,),
        in_specs=[pl.BlockSpec((1, rows, members), lambda t: (t, 0, 0)), pl.BlockSpec((1, members, members), lambda t: (t, 0, 0))],
        out_specs=pl.BlockSpec((1, rows, members), lambda t: (t, 0, 0)),
        cost_estimate=pl.CostEstimate(flops=2 * times * rows * members * members, transcendentals=0, bytes_accessed=2 * anomalies.size * 2 + suffix.size * 4),
    )(anomalies, suffix)


def on_device(anomalies, obs_weight):
    times_dev, rows_dev, members = anomalies.shape
    total_rows = rows_dev * lax.axis_size("state")
    weighted = (anomalies * obs_weight[:, :, None]).astype(jnp.bfloat16)
    partial_gram = jnp.einsum("trm,trn->tmn", weighted, weighted, preferred_element_type=jnp.float32)
    gram_sum = state_sum(partial_gram, "state")
    covariance = gram_sum / total_rows + jnp.eye(members, dtype=jnp.float32)
    transform = newton_root(covariance)
    local_product = transform[times_dev - 1]
    for time_index in range(times_dev - 2, -1, -1):
        local_product = jnp.matmul(transform[time_index], local_product, precision=HI)
    product = later_product(local_product, "tm")
    suffixes = []
    for time_index in range(times_dev - 1, -1, -1):
        product = jnp.matmul(transform[time_index], product, precision=HI)
        suffixes.append(product)
    suffix = jnp.stack(suffixes[::-1])
    if PALLAS_SMOOTH:
        smoothed = smooth(anomalies, suffix)
    else:
        smoothed = jnp.einsum("trm,tmn->trn", anomalies, suffix.astype(jnp.bfloat16), preferred_element_type=jnp.float32).astype(jnp.bfloat16)
    return (smoothed, suffix)


def solution(mesh):
    placed = (P("tm", "state", None), P("tm", "state"))
    return jax.shard_map(on_device, mesh=mesh, in_specs=placed, out_specs=(P("tm", "state", None), P("tm", None, None)), check_vma=False)
```

```python
import jax
import jax.numpy as jnp
from jax import lax
from jax.sharding import PartitionSpec as P
from jax.experimental import pallas as pl
from jax.experimental.layout import Layout, with_layout_constraint
from jax.experimental.pallas import tpu as pltpu

NS_STEPS = 4
HI = lax.Precision.HIGH
CHIP_RADIX = 4
SPLIT = True
PALLAS_SMOOTH = False


def radix_plan(count):
    plan, place = [], 1
    if count % 2 == 0 and count > 1:
        plan.append((2, 1))
        place = 2
    while place < count:
        radix = min(CHIP_RADIX, count // place)
        plan.append((radix, place))
        place *= radix
    return plan


def digit_pairs(count, radix, place, offset):
    pairs = []
    for source in range(count):
        digit = (source // place) % radix
        pairs.append((source, source + (((digit + offset) % radix) - digit) * place))
    return pairs


def grouped_sum(value, axis):
    count, me = lax.axis_size(axis), lax.axis_index(axis)
    plan = radix_plan(count)
    rows = value.shape[0]
    for radix, place in plan:
        digit = (me // place) % radix
        if radix == 2:
            upper = digit == 1
            half = value.shape[0] // 2
            low, high = value[:half], value[half:]
            send, keep = jnp.where(upper, low, high), jnp.where(upper, high, low)
            value = keep + lax.ppermute(send, axis, digit_pairs(count, radix, place, 1))
            continue
        chunk = value.shape[0] // radix
        pieces = value.reshape((radix, chunk) + value.shape[1:])
        total = lax.dynamic_index_in_dim(pieces, digit, 0, keepdims=False)
        for offset in range(1, radix):
            send = lax.dynamic_index_in_dim(pieces, (digit + offset) % radix, 0, keepdims=False)
            total = total + lax.ppermute(send, axis, digit_pairs(count, radix, place, offset))
        value = total
    for radix, place in plan[::-1]:
        digit = (me // place) % radix
        if radix == 2:
            other = lax.ppermute(value, axis, digit_pairs(count, radix, place, 1))
            value = jnp.where(digit == 1, jnp.concatenate([other, value]), jnp.concatenate([value, other]))
            continue
        got = [value] + [lax.ppermute(value, axis, digit_pairs(count, radix, place, offset)) for offset in range(1, radix)]
        stacked = jnp.stack(got)
        order = (digit - jnp.arange(radix)) % radix
        value = jnp.take(stacked, order, axis=0).reshape((radix * value.shape[0],) + value.shape[1:])
    return value


def state_sum(partial_gram, axis):
    times, n, _ = partial_gram.shape
    return grouped_sum(partial_gram.reshape(times * n, n), axis).reshape(times, n, n)


def newton_root(covariance):
    identity = jnp.eye(covariance.shape[-1], dtype=jnp.float32)
    row_bound = jnp.max(jnp.sum(jnp.abs(covariance), axis=-1), axis=-1)
    iterate = covariance / row_bound[:, None, None]
    inverse_root = jnp.broadcast_to(identity, covariance.shape)
    for sweep_index in range(NS_STEPS):
        factor = 1.5 * identity - 0.5 * jnp.matmul(inverse_root, iterate, precision=HI)
        iterate = jnp.matmul(iterate, factor, precision=HI)
        inverse_root = jnp.matmul(factor, inverse_root, precision=HI)
    return inverse_root / jnp.sqrt(row_bound)[:, None, None]


def split_shift(value, axis, pairs):
    count = lax.axis_size("state")
    if not SPLIT or count % 2:
        return lax.ppermute(value, axis, pairs)
    upper = lax.axis_index("state") % 2 == 1
    half = value.shape[0] // 2
    part = jnp.where(upper, value[half:], value[:half])
    got = lax.ppermute(part, axis, pairs)
    other = lax.ppermute(got, "state", digit_pairs(count, 2, 1, 1))
    return jnp.where(upper, jnp.concatenate([other, got]), jnp.concatenate([got, other]))


def later_product(local, axis):
    count, me = lax.axis_size(axis), lax.axis_index(axis)
    identity = jnp.eye(local.shape[-1], dtype=local.dtype)
    if count == 1:
        return identity
    shifted = split_shift(local, axis, [(j, j - 1) for j in range(1, count)])
    carried = jnp.where(me + 1 < count, shifted, identity)
    reach = 1
    while reach < count - 1:
        further = split_shift(carried, axis, [(j, j - reach) for j in range(reach, count)])
        further = jnp.where(me + reach < count, further, identity)
        carried = jnp.matmul(carried, further, precision=HI)
        reach *= 2
    return carried


def smooth_kernel(anomaly_ref, suffix_ref, out_ref):
    out_ref[0] = jnp.dot(anomaly_ref[0], suffix_ref[0].astype(jnp.bfloat16), preferred_element_type=jnp.float32).astype(out_ref.dtype)


def smooth(anomalies, suffix):
    times, rows, members = anomalies.shape
    return pl.pallas_call(
        smooth_kernel,
        out_shape=jax.ShapeDtypeStruct(anomalies.shape, anomalies.dtype),
        grid=(times,),
        in_specs=[pl.BlockSpec((1, rows, members), lambda t: (t, 0, 0)), pl.BlockSpec((1, members, members), lambda t: (t, 0, 0))],
        out_specs=pl.BlockSpec((1, rows, members), lambda t: (t, 0, 0)),
        cost_estimate=pl.CostEstimate(flops=2 * times * rows * members * members, transcendentals=0, bytes_accessed=2 * anomalies.size * 2 + suffix.size * 4),
    )(anomalies, suffix)


def on_device(anomalies, obs_weight):
    times_dev, rows_dev, members = anomalies.shape
    total_rows = rows_dev * lax.axis_size("state")
    weighted = (anomalies * obs_weight[:, :, None]).astype(jnp.bfloat16)
    partial_gram = jnp.einsum("trm,trn->tmn", weighted, weighted, preferred_element_type=jnp.float32)
    gram_sum = state_sum(partial_gram, "state")
    covariance = gram_sum / total_rows + jnp.eye(members, dtype=jnp.float32)
    transform = newton_root(covariance)
    local_product = transform[times_dev - 1]
    for time_index in range(times_dev - 2, -1, -1):
        local_product = jnp.matmul(transform[time_index], local_product, precision=HI)
    product = later_product(local_product, "tm")
    suffixes = []
    for time_index in range(times_dev - 1, -1, -1):
        product = jnp.matmul(transform[time_index], product, precision=HI)
        suffixes.append(product)
    suffix = jnp.stack(suffixes[::-1])
    if PALLAS_SMOOTH:
        smoothed = smooth(anomalies, suffix)
    else:
        smoothed = jnp.einsum("trm,tmn->trn", anomalies, suffix.astype(jnp.bfloat16), preferred_element_type=jnp.float32).astype(jnp.bfloat16)
        smoothed = with_layout_constraint(smoothed, Layout(major_to_minor=(0, 1, 2)))
    return (smoothed, suffix)


def solution(mesh):
    placed = (P("tm", "state", None), P("tm", "state"))
    return jax.shard_map(on_device, mesh=mesh, in_specs=placed, out_specs=(P("tm", "state", None), P("tm", None, None)), check_vma=False)
```

```python
import jax
import jax.numpy as jnp
from jax import lax
from jax.sharding import PartitionSpec as P
from jax.experimental import pallas as pl
from jax.experimental.layout import Layout, with_layout_constraint
from jax.experimental.pallas import tpu as pltpu

NS_STEPS = 4
HI = lax.Precision.HIGH
NS_PRECISION = lax.Precision.HIGH
CHIP_RADIX = 4
SPLIT = True
PALLAS_SMOOTH = False


def radix_plan(count):
    plan, place = [], 1
    if count % 2 == 0 and count > 1:
        plan.append((2, 1))
        place = 2
    while place < count:
        radix = min(CHIP_RADIX, count // place)
        plan.append((radix, place))
        place *= radix
    return plan


def digit_pairs(count, radix, place, offset):
    pairs = []
    for source in range(count):
        digit = (source // place) % radix
        pairs.append((source, source + (((digit + offset) % radix) - digit) * place))
    return pairs


def grouped_sum(value, axis):
    count, me = lax.axis_size(axis), lax.axis_index(axis)
    plan = radix_plan(count)
    rows = value.shape[0]
    for radix, place in plan:
        digit = (me // place) % radix
        if radix == 2:
            upper = digit == 1
            half = value.shape[0] // 2
            low, high = value[:half], value[half:]
            send, keep = jnp.where(upper, low, high), jnp.where(upper, high, low)
            value = keep + lax.ppermute(send, axis, digit_pairs(count, radix, place, 1))
            continue
        chunk = value.shape[0] // radix
        pieces = value.reshape((radix, chunk) + value.shape[1:])
        total = lax.dynamic_index_in_dim(pieces, digit, 0, keepdims=False)
        for offset in range(1, radix):
            send = lax.dynamic_index_in_dim(pieces, (digit + offset) % radix, 0, keepdims=False)
            total = total + lax.ppermute(send, axis, digit_pairs(count, radix, place, offset))
        value = total
    for radix, place in plan[::-1]:
        digit = (me // place) % radix
        if radix == 2:
            other = lax.ppermute(value, axis, digit_pairs(count, radix, place, 1))
            value = jnp.where(digit == 1, jnp.concatenate([other, value]), jnp.concatenate([value, other]))
            continue
        got = [value] + [lax.ppermute(value, axis, digit_pairs(count, radix, place, offset)) for offset in range(1, radix)]
        stacked = jnp.stack(got)
        order = (digit - jnp.arange(radix)) % radix
        value = jnp.take(stacked, order, axis=0).reshape((radix * value.shape[0],) + value.shape[1:])
    return value


def state_sum(partial_gram, axis):
    times, n, _ = partial_gram.shape
    return grouped_sum(partial_gram.reshape(times * n, n), axis).reshape(times, n, n)


def newton_root(covariance):
    identity = jnp.eye(covariance.shape[-1], dtype=jnp.float32)
    row_bound = jnp.max(jnp.sum(jnp.abs(covariance), axis=-1), axis=-1)
    iterate = covariance / row_bound[:, None, None]
    factor = 1.5 * identity - 0.5 * iterate
    pair = jnp.stack([jnp.matmul(iterate, factor, precision=NS_PRECISION), factor], axis=1)
    for sweep_index in range(NS_STEPS - 1):
        factor = 1.5 * identity - 0.5 * jnp.matmul(pair[:, 1], pair[:, 0], precision=NS_PRECISION)
        pair = jnp.einsum("tkij,tjl->tkil", pair, factor, precision=NS_PRECISION)
    return pair[:, 1] / jnp.sqrt(row_bound)[:, None, None]


def split_shift(value, axis, pairs):
    count = lax.axis_size("state")
    if not SPLIT or count % 2:
        return lax.ppermute(value, axis, pairs)
    upper = lax.axis_index("state") % 2 == 1
    half = value.shape[0] // 2
    part = jnp.where(upper, value[half:], value[:half])
    got = lax.ppermute(part, axis, pairs)
    other = lax.ppermute(got, "state", digit_pairs(count, 2, 1, 1))
    return jnp.where(upper, jnp.concatenate([other, got]), jnp.concatenate([got, other]))


def later_product(local, axis):
    count, me = lax.axis_size(axis), lax.axis_index(axis)
    identity = jnp.eye(local.shape[-1], dtype=local.dtype)
    if count == 1:
        return identity
    shifted = split_shift(local, axis, [(j, j - 1) for j in range(1, count)])
    carried = jnp.where(me + 1 < count, shifted, identity)
    reach = 1
    while reach < count - 1:
        further = split_shift(carried, axis, [(j, j - reach) for j in range(reach, count)])
        further = jnp.where(me + reach < count, further, identity)
        carried = jnp.matmul(carried, further, precision=HI)
        reach *= 2
    return carried


def smooth_kernel(anomaly_ref, suffix_ref, out_ref):
    out_ref[0] = jnp.dot(anomaly_ref[0], suffix_ref[0].astype(jnp.bfloat16), preferred_element_type=jnp.float32).astype(out_ref.dtype)


def smooth(anomalies, suffix):
    times, rows, members = anomalies.shape
    return pl.pallas_call(
        smooth_kernel,
        out_shape=jax.ShapeDtypeStruct(anomalies.shape, anomalies.dtype),
        grid=(times,),
        in_specs=[pl.BlockSpec((1, rows, members), lambda t: (t, 0, 0)), pl.BlockSpec((1, members, members), lambda t: (t, 0, 0))],
        out_specs=pl.BlockSpec((1, rows, members), lambda t: (t, 0, 0)),
        cost_estimate=pl.CostEstimate(flops=2 * times * rows * members * members, transcendentals=0, bytes_accessed=2 * anomalies.size * 2 + suffix.size * 4),
    )(anomalies, suffix)


def on_device(anomalies, obs_weight):
    times_dev, rows_dev, members = anomalies.shape
    total_rows = rows_dev * lax.axis_size("state")
    weighted = (anomalies * obs_weight[:, :, None]).astype(jnp.bfloat16)
    half = rows_dev // 2
    partial_gram = jnp.einsum("trm,trn->tmn", weighted[:, :half], weighted[:, :half], preferred_element_type=jnp.float32) + jnp.einsum("trm,trn->tmn", weighted[:, half:], weighted[:, half:], preferred_element_type=jnp.float32)
    gram_sum = state_sum(partial_gram, "state")
    covariance = gram_sum / total_rows + jnp.eye(members, dtype=jnp.float32)
    transform = newton_root(covariance)
    local_product = transform[times_dev - 1]
    for time_index in range(times_dev - 2, -1, -1):
        local_product = jnp.matmul(transform[time_index], local_product, precision=HI)
    product = later_product(local_product, "tm")
    suffixes = []
    for time_index in range(times_dev - 1, -1, -1):
        product = jnp.matmul(transform[time_index], product, precision=HI)
        suffixes.append(product)
    suffix = jnp.stack(suffixes[::-1])
    if PALLAS_SMOOTH:
        smoothed = smooth(anomalies, suffix)
    else:
        smoothed = jnp.einsum("trm,tmn->trn", anomalies, suffix.astype(jnp.bfloat16), preferred_element_type=jnp.float32).astype(jnp.bfloat16)
        smoothed = with_layout_constraint(smoothed, Layout(major_to_minor=(0, 1, 2)))
    return (smoothed, suffix)


def solution(mesh):
    placed = (P("tm", "state", None), P("tm", "state"))
    return jax.shard_map(on_device, mesh=mesh, in_specs=placed, out_specs=(P("tm", "state", None), P("tm", None, None)), check_vma=False)
```

```python
import jax
import jax.numpy as jnp
from jax import lax
from jax.sharding import PartitionSpec as P
from jax.experimental import pallas as pl
from jax.experimental.layout import Layout, with_layout_constraint
from jax.experimental.pallas import tpu as pltpu

NS_STEPS = 4
HI = lax.Precision.HIGH
NS_PRECISION = lax.Precision.HIGHEST
CHIP_RADIX = 4
SPLIT = True
PALLAS_SMOOTH = False


def radix_plan(count):
    plan, place = [], 1
    if count % 2 == 0 and count > 1:
        plan.append((2, 1))
        place = 2
    while place < count:
        radix = min(CHIP_RADIX, count // place)
        plan.append((radix, place))
        place *= radix
    return plan


def digit_pairs(count, radix, place, offset):
    pairs = []
    for source in range(count):
        digit = (source // place) % radix
        pairs.append((source, source + (((digit + offset) % radix) - digit) * place))
    return pairs


def grouped_sum(value, axis):
    count, me = lax.axis_size(axis), lax.axis_index(axis)
    plan = radix_plan(count)
    rows = value.shape[0]
    for radix, place in plan:
        digit = (me // place) % radix
        if radix == 2:
            upper = digit == 1
            half = value.shape[0] // 2
            low, high = value[:half], value[half:]
            send, keep = jnp.where(upper, low, high), jnp.where(upper, high, low)
            value = keep + lax.ppermute(send, axis, digit_pairs(count, radix, place, 1))
            continue
        chunk = value.shape[0] // radix
        pieces = value.reshape((radix, chunk) + value.shape[1:])
        total = lax.dynamic_index_in_dim(pieces, digit, 0, keepdims=False)
        for offset in range(1, radix):
            send = lax.dynamic_index_in_dim(pieces, (digit + offset) % radix, 0, keepdims=False)
            total = total + lax.ppermute(send, axis, digit_pairs(count, radix, place, offset))
        value = total
    for radix, place in plan[::-1]:
        digit = (me // place) % radix
        if radix == 2:
            other = lax.ppermute(value, axis, digit_pairs(count, radix, place, 1))
            value = jnp.where(digit == 1, jnp.concatenate([other, value]), jnp.concatenate([value, other]))
            continue
        got = [value] + [lax.ppermute(value, axis, digit_pairs(count, radix, place, offset)) for offset in range(1, radix)]
        stacked = jnp.stack(got)
        order = (digit - jnp.arange(radix)) % radix
        value = jnp.take(stacked, order, axis=0).reshape((radix * value.shape[0],) + value.shape[1:])
    return value


def state_sum(partial_gram, axis):
    times, n, _ = partial_gram.shape
    return grouped_sum(partial_gram.reshape(times * n, n), axis).reshape(times, n, n)


def newton_root(covariance):
    identity = jnp.eye(covariance.shape[-1], dtype=jnp.float32)
    row_bound = jnp.max(jnp.sum(jnp.abs(covariance), axis=-1), axis=-1)
    iterate = covariance / row_bound[:, None, None]
    factor = 1.5 * identity - 0.5 * iterate
    pair = jnp.stack([jnp.matmul(iterate, factor, precision=NS_PRECISION), factor], axis=1)
    for sweep_index in range(NS_STEPS - 1):
        factor = 1.5 * identity - 0.5 * jnp.matmul(pair[:, 1], pair[:, 0], precision=NS_PRECISION)
        pair = jnp.einsum("tkij,tjl->tkil", pair, factor, precision=NS_PRECISION)
    return pair[:, 1] / jnp.sqrt(row_bound)[:, None, None]


def split_shift(value, axis, pairs):
    count = lax.axis_size("state")
    if not SPLIT or count % 2:
        return lax.ppermute(value, axis, pairs)
    upper = lax.axis_index("state") % 2 == 1
    half = value.shape[0] // 2
    part = jnp.where(upper, value[half:], value[:half])
    got = lax.ppermute(part, axis, pairs)
    other = lax.ppermute(got, "state", digit_pairs(count, 2, 1, 1))
    return jnp.where(upper, jnp.concatenate([other, got]), jnp.concatenate([got, other]))


def later_product(local, axis):
    count, me = lax.axis_size(axis), lax.axis_index(axis)
    identity = jnp.eye(local.shape[-1], dtype=local.dtype)
    if count == 1:
        return identity
    shifted = split_shift(local, axis, [(j, j - 1) for j in range(1, count)])
    carried = jnp.where(me + 1 < count, shifted, identity)
    reach = 1
    while reach < count - 1:
        further = split_shift(carried, axis, [(j, j - reach) for j in range(reach, count)])
        further = jnp.where(me + reach < count, further, identity)
        carried = jnp.matmul(carried, further, precision=HI)
        reach *= 2
    return carried


def smooth_kernel(anomaly_ref, suffix_ref, out_ref):
    out_ref[0] = jnp.dot(anomaly_ref[0], suffix_ref[0].astype(jnp.bfloat16), preferred_element_type=jnp.float32).astype(out_ref.dtype)


def smooth(anomalies, suffix):
    times, rows, members = anomalies.shape
    return pl.pallas_call(
        smooth_kernel,
        out_shape=jax.ShapeDtypeStruct(anomalies.shape, anomalies.dtype),
        grid=(times,),
        in_specs=[pl.BlockSpec((1, rows, members), lambda t: (t, 0, 0)), pl.BlockSpec((1, members, members), lambda t: (t, 0, 0))],
        out_specs=pl.BlockSpec((1, rows, members), lambda t: (t, 0, 0)),
        cost_estimate=pl.CostEstimate(flops=2 * times * rows * members * members, transcendentals=0, bytes_accessed=2 * anomalies.size * 2 + suffix.size * 4),
    )(anomalies, suffix)


def on_device(anomalies, obs_weight):
    times_dev, rows_dev, members = anomalies.shape
    total_rows = rows_dev * lax.axis_size("state")
    weighted = (anomalies * obs_weight[:, :, None]).astype(jnp.bfloat16)
    half = rows_dev // 2
    partial_gram = jnp.einsum("trm,trn->tmn", weighted[:, :half], weighted[:, :half], preferred_element_type=jnp.float32) + jnp.einsum("trm,trn->tmn", weighted[:, half:], weighted[:, half:], preferred_element_type=jnp.float32)
    gram_sum = state_sum(partial_gram, "state")
    covariance = gram_sum / total_rows + jnp.eye(members, dtype=jnp.float32)
    transform = newton_root(covariance)
    local_product = transform[times_dev - 1]
    for time_index in range(times_dev - 2, -1, -1):
        local_product = jnp.matmul(transform[time_index], local_product, precision=HI)
    product = later_product(local_product, "tm")
    suffixes = []
    for time_index in range(times_dev - 1, -1, -1):
        product = jnp.matmul(transform[time_index], product, precision=HI)
        suffixes.append(product)
    suffix = jnp.stack(suffixes[::-1])
    if PALLAS_SMOOTH:
        smoothed = smooth(anomalies, suffix)
    else:
        smoothed = jnp.einsum("trm,tmn->trn", anomalies, suffix.astype(jnp.bfloat16), preferred_element_type=jnp.float32).astype(jnp.bfloat16)
        smoothed = with_layout_constraint(smoothed, Layout(major_to_minor=(0, 1, 2)))
    return (smoothed, suffix)


def solution(mesh):
    placed = (P("tm", "state", None), P("tm", "state"))
    return jax.shard_map(on_device, mesh=mesh, in_specs=placed, out_specs=(P("tm", "state", None), P("tm", None, None)), check_vma=False)
```

```python
import jax
import jax.numpy as jnp
from jax import lax
from jax.sharding import PartitionSpec as P
from jax.experimental import pallas as pl
from jax.experimental.layout import Layout, with_layout_constraint
from jax.experimental.pallas import tpu as pltpu

NS_STEPS = 4
HI = lax.Precision.HIGH
NS_PRECISION = lax.Precision.HIGH
CHIP_RADIX = 4
SPLIT = True
PALLAS_SMOOTH = False


def radix_plan(count):
    plan, place = [], 1
    if count % 2 == 0 and count > 1:
        plan.append((2, 1))
        place = 2
    while place < count:
        radix = min(CHIP_RADIX, count // place)
        plan.append((radix, place))
        place *= radix
    return plan


def digit_pairs(count, radix, place, offset):
    pairs = []
    for source in range(count):
        digit = (source // place) % radix
        pairs.append((source, source + (((digit + offset) % radix) - digit) * place))
    return pairs


def grouped_sum(value, axis):
    count, me = lax.axis_size(axis), lax.axis_index(axis)
    plan = radix_plan(count)
    rows = value.shape[0]
    for radix, place in plan:
        digit = (me // place) % radix
        if radix == 2:
            upper = digit == 1
            half = value.shape[0] // 2
            low, high = value[:half], value[half:]
            send, keep = jnp.where(upper, low, high), jnp.where(upper, high, low)
            value = keep + lax.ppermute(send, axis, digit_pairs(count, radix, place, 1))
            continue
        chunk = value.shape[0] // radix
        pieces = value.reshape((radix, chunk) + value.shape[1:])
        total = lax.dynamic_index_in_dim(pieces, digit, 0, keepdims=False)
        for offset in range(1, radix):
            send = lax.dynamic_index_in_dim(pieces, (digit + offset) % radix, 0, keepdims=False)
            total = total + lax.ppermute(send, axis, digit_pairs(count, radix, place, offset))
        value = total
    for radix, place in plan[::-1]:
        digit = (me // place) % radix
        if radix == 2:
            other = lax.ppermute(value, axis, digit_pairs(count, radix, place, 1))
            value = jnp.where(digit == 1, jnp.concatenate([other, value]), jnp.concatenate([value, other]))
            continue
        got = [value] + [lax.ppermute(value, axis, digit_pairs(count, radix, place, offset)) for offset in range(1, radix)]
        stacked = jnp.stack(got)
        order = (digit - jnp.arange(radix)) % radix
        value = jnp.take(stacked, order, axis=0).reshape((radix * value.shape[0],) + value.shape[1:])
    return value


def state_sum(partial_gram, axis):
    times, n, _ = partial_gram.shape
    return grouped_sum(partial_gram.reshape(times * n, n), axis).reshape(times, n, n)


def newton_root(covariance):
    identity = jnp.eye(covariance.shape[-1], dtype=jnp.float32)
    row_bound = jnp.max(jnp.sum(jnp.abs(covariance), axis=-1), axis=-1)
    iterate = covariance / row_bound[:, None, None]
    factor = 1.5 * identity - 0.5 * iterate
    pair = jnp.stack([jnp.matmul(iterate, factor, precision=NS_PRECISION), factor], axis=1)
    for sweep_index in range(NS_STEPS - 1):
        precision = lax.Precision.HIGHEST if sweep_index == NS_STEPS - 2 else NS_PRECISION
        factor = 1.5 * identity - 0.5 * jnp.matmul(pair[:, 1], pair[:, 0], precision=precision)
        pair = jnp.einsum("tkij,tjl->tkil", pair, factor, precision=precision)
    return pair[:, 1] / jnp.sqrt(row_bound)[:, None, None]


def split_shift(value, axis, pairs):
    count = lax.axis_size("state")
    if not SPLIT or count % 2:
        return lax.ppermute(value, axis, pairs)
    upper = lax.axis_index("state") % 2 == 1
    half = value.shape[0] // 2
    part = jnp.where(upper, value[half:], value[:half])
    got = lax.ppermute(part, axis, pairs)
    other = lax.ppermute(got, "state", digit_pairs(count, 2, 1, 1))
    return jnp.where(upper, jnp.concatenate([other, got]), jnp.concatenate([got, other]))


def later_product(local, axis):
    count, me = lax.axis_size(axis), lax.axis_index(axis)
    identity = jnp.eye(local.shape[-1], dtype=local.dtype)
    if count == 1:
        return identity
    shifted = split_shift(local, axis, [(j, j - 1) for j in range(1, count)])
    carried = jnp.where(me + 1 < count, shifted, identity)
    reach = 1
    while reach < count - 1:
        further = split_shift(carried, axis, [(j, j - reach) for j in range(reach, count)])
        further = jnp.where(me + reach < count, further, identity)
        carried = jnp.matmul(carried, further, precision=HI)
        reach *= 2
    return carried


def smooth_kernel(anomaly_ref, suffix_ref, out_ref):
    out_ref[0] = jnp.dot(anomaly_ref[0], suffix_ref[0].astype(jnp.bfloat16), preferred_element_type=jnp.float32).astype(out_ref.dtype)


def smooth(anomalies, suffix):
    times, rows, members = anomalies.shape
    return pl.pallas_call(
        smooth_kernel,
        out_shape=jax.ShapeDtypeStruct(anomalies.shape, anomalies.dtype),
        grid=(times,),
        in_specs=[pl.BlockSpec((1, rows, members), lambda t: (t, 0, 0)), pl.BlockSpec((1, members, members), lambda t: (t, 0, 0))],
        out_specs=pl.BlockSpec((1, rows, members), lambda t: (t, 0, 0)),
        cost_estimate=pl.CostEstimate(flops=2 * times * rows * members * members, transcendentals=0, bytes_accessed=2 * anomalies.size * 2 + suffix.size * 4),
    )(anomalies, suffix)


def on_device(anomalies, obs_weight):
    times_dev, rows_dev, members = anomalies.shape
    total_rows = rows_dev * lax.axis_size("state")
    weighted = (anomalies * obs_weight[:, :, None]).astype(jnp.bfloat16)
    half = rows_dev // 2
    partial_gram = jnp.einsum("trm,trn->tmn", weighted[:, :half], weighted[:, :half], preferred_element_type=jnp.float32) + jnp.einsum("trm,trn->tmn", weighted[:, half:], weighted[:, half:], preferred_element_type=jnp.float32)
    gram_sum = state_sum(partial_gram, "state")
    covariance = gram_sum / total_rows + jnp.eye(members, dtype=jnp.float32)
    transform = newton_root(covariance)
    local_product = transform[times_dev - 1]
    for time_index in range(times_dev - 2, -1, -1):
        local_product = jnp.matmul(transform[time_index], local_product, precision=HI)
    product = later_product(local_product, "tm")
    suffixes = []
    for time_index in range(times_dev - 1, -1, -1):
        product = jnp.matmul(transform[time_index], product, precision=HI)
        suffixes.append(product)
    suffix = jnp.stack(suffixes[::-1])
    if PALLAS_SMOOTH:
        smoothed = smooth(anomalies, suffix)
    else:
        smoothed = jnp.einsum("trm,tmn->trn", anomalies, suffix.astype(jnp.bfloat16), preferred_element_type=jnp.float32).astype(jnp.bfloat16)
        smoothed = with_layout_constraint(smoothed, Layout(major_to_minor=(0, 1, 2)))
    return (smoothed, suffix)


def solution(mesh):
    placed = (P("tm", "state", None), P("tm", "state"))
    return jax.shard_map(on_device, mesh=mesh, in_specs=placed, out_specs=(P("tm", "state", None), P("tm", None, None)), check_vma=False)
```

```python
import jax
import jax.numpy as jnp
from jax import lax
from jax.sharding import PartitionSpec as P
from jax.experimental import pallas as pl
from jax.experimental.layout import Layout, with_layout_constraint
from jax.experimental.pallas import tpu as pltpu

NS_STEPS = 4
HI = lax.Precision.HIGH
NS_PRECISION = lax.Precision.HIGH
CHIP_RADIX = 4
SPLIT = True
PALLAS_SMOOTH = False


def radix_plan(count):
    plan, place = [], 1
    if count % 2 == 0 and count > 1:
        plan.append((2, 1))
        place = 2
    while place < count:
        radix = min(CHIP_RADIX, count // place)
        plan.append((radix, place))
        place *= radix
    return plan


def digit_pairs(count, radix, place, offset):
    pairs = []
    for source in range(count):
        digit = (source // place) % radix
        pairs.append((source, source + (((digit + offset) % radix) - digit) * place))
    return pairs


def grouped_sum(value, axis):
    count, me = lax.axis_size(axis), lax.axis_index(axis)
    plan = radix_plan(count)
    rows = value.shape[0]
    for radix, place in plan:
        digit = (me // place) % radix
        if radix == 2:
            upper = digit == 1
            half = value.shape[0] // 2
            low, high = value[:half], value[half:]
            send, keep = jnp.where(upper, low, high), jnp.where(upper, high, low)
            value = keep + lax.ppermute(send, axis, digit_pairs(count, radix, place, 1))
            continue
        chunk = value.shape[0] // radix
        pieces = value.reshape((radix, chunk) + value.shape[1:])
        total = lax.dynamic_index_in_dim(pieces, digit, 0, keepdims=False)
        for offset in range(1, radix):
            send = lax.dynamic_index_in_dim(pieces, (digit + offset) % radix, 0, keepdims=False)
            total = total + lax.ppermute(send, axis, digit_pairs(count, radix, place, offset))
        value = total
    for radix, place in plan[::-1]:
        digit = (me // place) % radix
        if radix == 2:
            other = lax.ppermute(value, axis, digit_pairs(count, radix, place, 1))
            value = jnp.where(digit == 1, jnp.concatenate([other, value]), jnp.concatenate([value, other]))
            continue
        got = [value] + [lax.ppermute(value, axis, digit_pairs(count, radix, place, offset)) for offset in range(1, radix)]
        placed = []
        for k in range(radix):
            source = (digit - k) % radix
            piece = got[0]
            for offset in range(1, radix):
                piece = jnp.where(source == offset, got[offset], piece)
            placed.append(piece)
        value = jnp.concatenate(placed)
    return value


def state_sum(partial_gram, axis):
    times, n, _ = partial_gram.shape
    return grouped_sum(partial_gram.reshape(times * n, n), axis).reshape(times, n, n)


def newton_root(covariance):
    identity = jnp.eye(covariance.shape[-1], dtype=jnp.float32)
    row_bound = jnp.max(jnp.sum(jnp.abs(covariance), axis=-1), axis=-1)
    iterate = covariance / row_bound[:, None, None]
    factor = 1.5 * identity - 0.5 * iterate
    pair = jnp.stack([jnp.matmul(iterate, factor, precision=NS_PRECISION), factor], axis=1)
    for sweep_index in range(NS_STEPS - 1):
        factor = 1.5 * identity - 0.5 * jnp.matmul(pair[:, 1], pair[:, 0], precision=NS_PRECISION)
        pair = jnp.einsum("tkij,tjl->tkil", pair, factor, precision=NS_PRECISION)
    return pair[:, 1] / jnp.sqrt(row_bound)[:, None, None]


def split_shift(value, axis, pairs):
    count = lax.axis_size("state")
    if not SPLIT or count % 2:
        return lax.ppermute(value, axis, pairs)
    upper = lax.axis_index("state") % 2 == 1
    half = value.shape[0] // 2
    part = jnp.where(upper, value[half:], value[:half])
    got = lax.ppermute(part, axis, pairs)
    other = lax.ppermute(got, "state", digit_pairs(count, 2, 1, 1))
    return jnp.where(upper, jnp.concatenate([other, got]), jnp.concatenate([got, other]))


def later_product(local, axis):
    count, me = lax.axis_size(axis), lax.axis_index(axis)
    identity = jnp.eye(local.shape[-1], dtype=local.dtype)
    if count == 1:
        return identity
    shifted = split_shift(local, axis, [(j, j - 1) for j in range(1, count)])
    carried = jnp.where(me + 1 < count, shifted, identity)
    reach = 1
    while reach < count - 1:
        further = split_shift(carried, axis, [(j, j - reach) for j in range(reach, count)])
        further = jnp.where(me + reach < count, further, identity)
        carried = jnp.matmul(carried, further, precision=HI)
        reach *= 2
    return carried


def smooth_kernel(anomaly_ref, suffix_ref, out_ref):
    out_ref[0] = jnp.dot(anomaly_ref[0], suffix_ref[0].astype(jnp.bfloat16), preferred_element_type=jnp.float32).astype(out_ref.dtype)


def smooth(anomalies, suffix):
    times, rows, members = anomalies.shape
    return pl.pallas_call(
        smooth_kernel,
        out_shape=jax.ShapeDtypeStruct(anomalies.shape, anomalies.dtype),
        grid=(times,),
        in_specs=[pl.BlockSpec((1, rows, members), lambda t: (t, 0, 0)), pl.BlockSpec((1, members, members), lambda t: (t, 0, 0))],
        out_specs=pl.BlockSpec((1, rows, members), lambda t: (t, 0, 0)),
        cost_estimate=pl.CostEstimate(flops=2 * times * rows * members * members, transcendentals=0, bytes_accessed=2 * anomalies.size * 2 + suffix.size * 4),
    )(anomalies, suffix)


def on_device(anomalies, obs_weight):
    times_dev, rows_dev, members = anomalies.shape
    total_rows = rows_dev * lax.axis_size("state")
    weighted = (anomalies * obs_weight[:, :, None]).astype(jnp.bfloat16)
    half = rows_dev // 2
    partial_gram = jnp.einsum("trm,trn->tmn", weighted[:, :half], weighted[:, :half], preferred_element_type=jnp.float32) + jnp.einsum("trm,trn->tmn", weighted[:, half:], weighted[:, half:], preferred_element_type=jnp.float32)
    gram_sum = state_sum(partial_gram, "state")
    covariance = gram_sum / total_rows + jnp.eye(members, dtype=jnp.float32)
    transform = newton_root(covariance)
    local_product = transform[times_dev - 1]
    for time_index in range(times_dev - 2, -1, -1):
        local_product = jnp.matmul(transform[time_index], local_product, precision=HI)
    product = later_product(local_product, "tm")
    suffixes = []
    for time_index in range(times_dev - 1, -1, -1):
        product = jnp.matmul(transform[time_index], product, precision=HI)
        suffixes.append(product)
    suffix = jnp.stack(suffixes[::-1])
    if PALLAS_SMOOTH:
        smoothed = smooth(anomalies, suffix)
    else:
        smoothed = jnp.einsum("trm,tmn->trn", anomalies, suffix.astype(jnp.bfloat16), preferred_element_type=jnp.float32).astype(jnp.bfloat16)
        smoothed = with_layout_constraint(smoothed, Layout(major_to_minor=(0, 1, 2)))
    return (smoothed, suffix)


def solution(mesh):
    placed = (P("tm", "state", None), P("tm", "state"))
    return jax.shard_map(on_device, mesh=mesh, in_specs=placed, out_specs=(P("tm", "state", None), P("tm", None, None)), check_vma=False)
```

```python
import jax
import jax.numpy as jnp
from jax import lax
from jax.sharding import PartitionSpec as P
from jax.experimental import pallas as pl
from jax.experimental.layout import Layout, with_layout_constraint
from jax.experimental.pallas import tpu as pltpu

NS_STEPS = 4
HI = lax.Precision.HIGH
NS_PRECISION = lax.Precision.HIGH
CHIP_RADIX = 4
SPLIT = True
PALLAS_SMOOTH = False


def radix_plan(count):
    plan, place = [], 1
    if count % 2 == 0 and count > 1:
        plan.append((2, 1))
        place = 2
    while place < count:
        radix = min(CHIP_RADIX, count // place)
        plan.append((radix, place))
        place *= radix
    return plan


def digit_pairs(count, radix, place, offset):
    pairs = []
    for source in range(count):
        digit = (source // place) % radix
        pairs.append((source, source + (((digit + offset) % radix) - digit) * place))
    return pairs


def grouped_sum(value, axis):
    count, me = lax.axis_size(axis), lax.axis_index(axis)
    plan = radix_plan(count)
    rows = value.shape[0]
    for radix, place in plan:
        digit = (me // place) % radix
        if radix == 2:
            upper = digit == 1
            half = value.shape[0] // 2
            low, high = value[:half], value[half:]
            send, keep = jnp.where(upper, low, high), jnp.where(upper, high, low)
            value = keep + lax.ppermute(send, axis, digit_pairs(count, radix, place, 1))
            continue
        chunk = value.shape[0] // radix
        pieces = value.reshape((radix, chunk) + value.shape[1:])
        total = lax.dynamic_index_in_dim(pieces, digit, 0, keepdims=False)
        for offset in range(1, radix):
            send = lax.dynamic_index_in_dim(pieces, (digit + offset) % radix, 0, keepdims=False)
            total = total + lax.ppermute(send, axis, digit_pairs(count, radix, place, offset))
        value = total
    for radix, place in plan[::-1]:
        digit = (me // place) % radix
        if radix == 2:
            other = lax.ppermute(value, axis, digit_pairs(count, radix, place, 1))
            value = jnp.where(digit == 1, jnp.concatenate([other, value]), jnp.concatenate([value, other]))
            continue
        got = [value] + [lax.ppermute(value, axis, digit_pairs(count, radix, place, offset)) for offset in range(1, radix)]
        placed = []
        for k in range(radix):
            source = (digit - k) % radix
            piece = got[0]
            for offset in range(1, radix):
                piece = jnp.where(source == offset, got[offset], piece)
            placed.append(piece)
        value = jnp.concatenate(placed)
    return value


def state_sum(partial_gram, axis):
    times, n, _ = partial_gram.shape
    return grouped_sum(partial_gram.reshape(times * n, n), axis).reshape(times, n, n)


def newton_root(covariance):
    identity = jnp.eye(covariance.shape[-1], dtype=jnp.float32)
    row_bound = jnp.max(jnp.sum(jnp.abs(covariance), axis=-1), axis=-1)
    iterate = covariance / row_bound[:, None, None]
    factor = 1.5 * identity - 0.5 * iterate
    pair = jnp.stack([jnp.matmul(iterate, factor, precision=NS_PRECISION), factor], axis=1)
    for sweep_index in range(NS_STEPS - 1):
        precision = lax.Precision.HIGHEST if sweep_index == NS_STEPS - 2 else NS_PRECISION
        factor = 1.5 * identity - 0.5 * jnp.matmul(pair[:, 1], pair[:, 0], precision=precision)
        pair = jnp.einsum("tkij,tjl->tkil", pair, factor, precision=precision)
    return pair[:, 1] / jnp.sqrt(row_bound)[:, None, None]


def split_shift(value, axis, pairs):
    count = lax.axis_size("state")
    if not SPLIT or count % 2:
        return lax.ppermute(value, axis, pairs)
    upper = lax.axis_index("state") % 2 == 1
    half = value.shape[0] // 2
    part = jnp.where(upper, value[half:], value[:half])
    got = lax.ppermute(part, axis, pairs)
    other = lax.ppermute(got, "state", digit_pairs(count, 2, 1, 1))
    return jnp.where(upper, jnp.concatenate([other, got]), jnp.concatenate([got, other]))


def later_product(local, axis):
    count, me = lax.axis_size(axis), lax.axis_index(axis)
    identity = jnp.eye(local.shape[-1], dtype=local.dtype)
    if count == 1:
        return identity
    shifted = split_shift(local, axis, [(j, j - 1) for j in range(1, count)])
    carried = jnp.where(me + 1 < count, shifted, identity)
    reach = 1
    while reach < count - 1:
        further = split_shift(carried, axis, [(j, j - reach) for j in range(reach, count)])
        further = jnp.where(me + reach < count, further, identity)
        carried = jnp.matmul(carried, further, precision=HI)
        reach *= 2
    return carried


def smooth_kernel(anomaly_ref, suffix_ref, out_ref):
    out_ref[0] = jnp.dot(anomaly_ref[0], suffix_ref[0].astype(jnp.bfloat16), preferred_element_type=jnp.float32).astype(out_ref.dtype)


def smooth(anomalies, suffix):
    times, rows, members = anomalies.shape
    return pl.pallas_call(
        smooth_kernel,
        out_shape=jax.ShapeDtypeStruct(anomalies.shape, anomalies.dtype),
        grid=(times,),
        in_specs=[pl.BlockSpec((1, rows, members), lambda t: (t, 0, 0)), pl.BlockSpec((1, members, members), lambda t: (t, 0, 0))],
        out_specs=pl.BlockSpec((1, rows, members), lambda t: (t, 0, 0)),
        cost_estimate=pl.CostEstimate(flops=2 * times * rows * members * members, transcendentals=0, bytes_accessed=2 * anomalies.size * 2 + suffix.size * 4),
    )(anomalies, suffix)


def on_device(anomalies, obs_weight):
    times_dev, rows_dev, members = anomalies.shape
    total_rows = rows_dev * lax.axis_size("state")
    weighted = (anomalies * obs_weight[:, :, None]).astype(jnp.bfloat16)
    half = rows_dev // 2
    partial_gram = jnp.einsum("trm,trn->tmn", weighted[:, :half], weighted[:, :half], preferred_element_type=jnp.float32) + jnp.einsum("trm,trn->tmn", weighted[:, half:], weighted[:, half:], preferred_element_type=jnp.float32)
    gram_sum = state_sum(partial_gram, "state")
    covariance = gram_sum / total_rows + jnp.eye(members, dtype=jnp.float32)
    transform = newton_root(covariance)
    local_product = transform[times_dev - 1]
    for time_index in range(times_dev - 2, -1, -1):
        local_product = jnp.matmul(transform[time_index], local_product, precision=HI)
    product = later_product(local_product, "tm")
    suffixes = []
    for time_index in range(times_dev - 1, -1, -1):
        product = jnp.matmul(transform[time_index], product, precision=HI)
        suffixes.append(product)
    suffix = jnp.stack(suffixes[::-1])
    if PALLAS_SMOOTH:
        smoothed = smooth(anomalies, suffix)
    else:
        smoothed = jnp.einsum("trm,tmn->trn", anomalies, suffix.astype(jnp.bfloat16), preferred_element_type=jnp.float32).astype(jnp.bfloat16)
        smoothed = with_layout_constraint(smoothed, Layout(major_to_minor=(0, 1, 2)))
    return (smoothed, suffix)


def solution(mesh):
    placed = (P("tm", "state", None), P("tm", "state"))
    return jax.shard_map(on_device, mesh=mesh, in_specs=placed, out_specs=(P("tm", "state", None), P("tm", None, None)), check_vma=False)
```

```python
import jax
import jax.numpy as jnp
from jax import lax
from jax.sharding import PartitionSpec as P
from jax.experimental import pallas as pl
from jax.experimental.layout import Layout, with_layout_constraint
from jax.experimental.pallas import tpu as pltpu

NS_STEPS = 4
HI = lax.Precision.HIGH
NS_PRECISION = lax.Precision.HIGH
CHIP_RADIX = 4
SPLIT = True
PALLAS_SMOOTH = False


def radix_plan(count):
    plan, place = [], 1
    if count % 2 == 0 and count > 1:
        plan.append((2, 1))
        place = 2
    while place < count:
        radix = min(CHIP_RADIX, count // place)
        plan.append((radix, place))
        place *= radix
    return plan


def digit_pairs(count, radix, place, offset):
    pairs = []
    for source in range(count):
        digit = (source // place) % radix
        pairs.append((source, source + (((digit + offset) % radix) - digit) * place))
    return pairs


def grouped_sum(value, axis):
    count, me = lax.axis_size(axis), lax.axis_index(axis)
    plan = radix_plan(count)
    rows = value.shape[0]
    for radix, place in plan:
        digit = (me // place) % radix
        if radix == 2:
            upper = digit == 1
            half = value.shape[0] // 2
            low, high = value[:half], value[half:]
            send, keep = jnp.where(upper, low, high), jnp.where(upper, high, low)
            value = keep + lax.ppermute(send, axis, digit_pairs(count, radix, place, 1))
            continue
        chunk = value.shape[0] // radix
        pieces = value.reshape((radix, chunk) + value.shape[1:])
        total = lax.dynamic_index_in_dim(pieces, digit, 0, keepdims=False)
        for offset in range(1, radix):
            send = lax.dynamic_index_in_dim(pieces, (digit + offset) % radix, 0, keepdims=False)
            total = total + lax.ppermute(send, axis, digit_pairs(count, radix, place, offset))
        value = total
    for radix, place in plan[::-1]:
        digit = (me // place) % radix
        if radix == 2:
            other = lax.ppermute(value, axis, digit_pairs(count, radix, place, 1))
            upper = digit == 1
            value = jnp.concatenate([jnp.where(upper, other, value), jnp.where(upper, value, other)])
            continue
        got = [value] + [lax.ppermute(value, axis, digit_pairs(count, radix, place, offset)) for offset in range(1, radix)]
        placed = []
        for k in range(radix):
            source = (digit - k) % radix
            piece = got[0]
            for offset in range(1, radix):
                piece = jnp.where(source == offset, got[offset], piece)
            placed.append(piece)
        value = jnp.concatenate(placed)
    return value


def state_sum(partial_gram, axis):
    times, n, _ = partial_gram.shape
    return grouped_sum(partial_gram.reshape(times * n, n), axis).reshape(times, n, n)


def newton_root(covariance):
    identity = jnp.eye(covariance.shape[-1], dtype=jnp.float32)
    row_bound = jnp.max(jnp.sum(jnp.abs(covariance), axis=-1), axis=-1)
    iterate = covariance / row_bound[:, None, None]
    factor = 1.5 * identity - 0.5 * iterate
    pair = jnp.stack([jnp.matmul(iterate, factor, precision=NS_PRECISION), factor], axis=1)
    for sweep_index in range(NS_STEPS - 1):
        precision = lax.Precision.HIGHEST if sweep_index == NS_STEPS - 2 else NS_PRECISION
        factor = 1.5 * identity - 0.5 * jnp.matmul(pair[:, 1], pair[:, 0], precision=precision)
        pair = jnp.einsum("tkij,tjl->tkil", pair, factor, precision=precision)
    return pair[:, 1] / jnp.sqrt(row_bound)[:, None, None]


def split_shift(value, axis, pairs):
    count = lax.axis_size("state")
    if not SPLIT or count % 2:
        return lax.ppermute(value, axis, pairs)
    upper = lax.axis_index("state") % 2 == 1
    half = value.shape[0] // 2
    part = jnp.where(upper, value[half:], value[:half])
    got = lax.ppermute(part, axis, pairs)
    other = lax.ppermute(got, "state", digit_pairs(count, 2, 1, 1))
    return jnp.concatenate([jnp.where(upper, other, got), jnp.where(upper, got, other)])


def later_product(local, axis):
    count, me = lax.axis_size(axis), lax.axis_index(axis)
    identity = jnp.eye(local.shape[-1], dtype=local.dtype)
    if count == 1:
        return identity
    shifted = split_shift(local, axis, [(j, j - 1) for j in range(1, count)])
    carried = jnp.where(me + 1 < count, shifted, identity)
    reach = 1
    while reach < count - 1:
        further = split_shift(carried, axis, [(j, j - reach) for j in range(reach, count)])
        further = jnp.where(me + reach < count, further, identity)
        carried = jnp.matmul(carried, further, precision=HI)
        reach *= 2
    return carried


def smooth_kernel(anomaly_ref, suffix_ref, out_ref):
    out_ref[0] = jnp.dot(anomaly_ref[0], suffix_ref[0].astype(jnp.bfloat16), preferred_element_type=jnp.float32).astype(out_ref.dtype)


def smooth(anomalies, suffix):
    times, rows, members = anomalies.shape
    return pl.pallas_call(
        smooth_kernel,
        out_shape=jax.ShapeDtypeStruct(anomalies.shape, anomalies.dtype),
        grid=(times,),
        in_specs=[pl.BlockSpec((1, rows, members), lambda t: (t, 0, 0)), pl.BlockSpec((1, members, members), lambda t: (t, 0, 0))],
        out_specs=pl.BlockSpec((1, rows, members), lambda t: (t, 0, 0)),
        cost_estimate=pl.CostEstimate(flops=2 * times * rows * members * members, transcendentals=0, bytes_accessed=2 * anomalies.size * 2 + suffix.size * 4),
    )(anomalies, suffix)


def on_device(anomalies, obs_weight):
    times_dev, rows_dev, members = anomalies.shape
    total_rows = rows_dev * lax.axis_size("state")
    weighted = (anomalies * obs_weight[:, :, None]).astype(jnp.bfloat16)
    half = rows_dev // 2
    partial_gram = jnp.einsum("trm,trn->tmn", weighted[:, :half], weighted[:, :half], preferred_element_type=jnp.float32) + jnp.einsum("trm,trn->tmn", weighted[:, half:], weighted[:, half:], preferred_element_type=jnp.float32)
    gram_sum = state_sum(partial_gram, "state")
    covariance = gram_sum / total_rows + jnp.eye(members, dtype=jnp.float32)
    transform = newton_root(covariance)
    local_product = transform[times_dev - 1]
    for time_index in range(times_dev - 2, -1, -1):
        local_product = jnp.matmul(transform[time_index], local_product, precision=HI)
    product = later_product(local_product, "tm")
    suffixes = []
    for time_index in range(times_dev - 1, -1, -1):
        product = jnp.matmul(transform[time_index], product, precision=HI)
        suffixes.append(product)
    suffix = jnp.stack(suffixes[::-1])
    if PALLAS_SMOOTH:
        smoothed = smooth(anomalies, suffix)
    else:
        smoothed = jnp.einsum("trm,tmn->trn", anomalies, suffix.astype(jnp.bfloat16), preferred_element_type=jnp.float32).astype(jnp.bfloat16)
        smoothed = with_layout_constraint(smoothed, Layout(major_to_minor=(0, 1, 2)))
    return (smoothed, suffix)


def solution(mesh):
    placed = (P("tm", "state", None), P("tm", "state"))
    return jax.shard_map(on_device, mesh=mesh, in_specs=placed, out_specs=(P("tm", "state", None), P("tm", None, None)), check_vma=False)
```
